32 devices in a mesh: row: 4 (over x, core), col: 8 (over z, y).
Axes of the slice: x: 2, y: 2, z: 4, core: 2. Of those that a mesh axis runs over, the one named last changes fastest.
Arguments:
- amplitudes: float32 [8, 64, 512, 512], P(None, None, None, ('row', 'col')), may hold values from -6 to 6
- cycle_integrals: float32 [64, 512, 4, 512], P('col'), may hold values from -0.125 to 0.125
- occ_irrep: int32 [64], replicated, may hold values from 0 to 7
- virt_irrep: int32 [512], replicated, may hold values from 0 to 7
Outputs:
- cycle: float32 [8, 512, 2048], P(None, 'row', 'col')
The draws below stay inside these ranges and needn't reach their ends.
All inputs are finite; a program needn't handle non-finite values.
Results may differ from the reference program's by a relative error of at most 0.0003.
Values sent between devices are 32-bit elements; how exact they have to be, the bound alone decides.
No kernel may reach another device: no remote copies, remote signals or barrier semaphores. Data moves between devices by JAX's collectives and lax.ppermute only.
A program may use at most 256 MiB of HBM per device.

```python
import jax
import jax.numpy as jnp
from jax import lax

O = 64
V = 512
I = 8
J = 4


def touch_ends(entries, rng, low, top_value):
    place = [jax.random.randint(jax.random.fold_in(rng, axis), (), 0, length) for axis, length in enumerate(entries.shape)]
    main_axis = entries.shape.index(max(entries.shape))
    beside = place[:main_axis] + [(place[main_axis] + 1) % entries.shape[main_axis]] + place[main_axis + 1:]
    return entries.at[tuple(place)].set(low).at[tuple(beside)].set(top_value)


def strengthened(array, own_key, source, target, shards_of, factor):
    def block_of(position):
        return (jnp.arange(array.shape[position]) // (array.shape[position] // shards_of)).reshape((-1,) + (1,) * (array.ndim - 1 - position))

    near = jax.random.permutation(own_key, shards_of)[block_of(target)]
    second = (block_of(target) + shards_of // 2) % shards_of
    return jnp.where((block_of(source) == near) | (block_of(source) == second), factor * array, array)


def block_scale(own_key, dims, cuts, least, high):
    loudness, own = 1.0, jax.random.fold_in(own_key, 6)
    for axis_at, shards_of in cuts:
        steps = jnp.exp(jax.random.uniform(jax.random.fold_in(own, axis_at), (shards_of,), jnp.float32, least / len(cuts), high / len(cuts)))
        loudness = loudness * jnp.repeat(steps, dims[axis_at] // shards_of).reshape([-1 if axis == axis_at else 1 for axis in range(len(dims))])
    return loudness


def bell_draw(rng, extent, spread, bound, pieces=(), kind=jnp.bfloat16):
    result = jax.random.normal(rng, extent, jnp.float32) * spread
    if len(pieces) > 0:
        result = block_scale(rng, extent, pieces, -0.22, 0.18) * result
    return jnp.clip(result, min=-bound, max=bound).astype(kind)


def heavy_noise(rng, extent, width, reach, shards, heavy, dtype=jnp.bfloat16):
    values = width * jax.random.normal(rng, extent, jnp.float32)
    if shards:
        values = values * block_scale(rng, extent, shards, -0.22, 0.18)
    return jnp.clip(strengthened(values, jax.random.fold_in(rng, 3), *heavy), -reach, reach).astype(dtype)


def setup_inputs(seed: int = 0) -> dict:
    key_list = jax.random.split(jax.random.key(seed), 5)
    amplitudes = bell_draw(key_list[0], (I, O, V, V), 1.0, 6.0, ((3, 32),), jnp.float32)
    cycle_integrals = heavy_noise(key_list[1], (O, V, J, V), (O * V // 8) ** -0.5, 0.125, ((0, 8),), (0, 3, 8, 2.0), jnp.float32)
    occ_irrep = touch_ends(jax.random.randint(key_list[2], (O,), 0, 8), jax.random.fold_in(key_list[2], 1), 0, 7).astype(jnp.int32)
    virt_irrep = touch_ends(jax.random.randint(key_list[3], (V,), 0, 8), jax.random.fold_in(key_list[3], 1), 0, 7).astype(jnp.int32)
    return {"amplitudes": amplitudes, "cycle_integrals": cycle_integrals, "occ_irrep": occ_irrep, "virt_irrep": virt_irrep}


def reference(amplitudes, cycle_integrals, occ_irrep, virt_irrep):
    slab_irrep = occ_irrep[:I]
    column_irrep = occ_irrep[:J]
    int_sym = (occ_irrep[:, None, None, None] ^ virt_irrep[None, :, None, None]) ^ (column_irrep[None, None, :, None] ^ virt_irrep[None, None, None, :])
    masked_ints = jnp.where(int_sym == 0, cycle_integrals, 0.0)

    def one_row(pair):
        row_amps, row_irrep = pair
        amp_sym = (row_irrep ^ occ_irrep[:, None, None]) ^ (virt_irrep[None, :, None] ^ virt_irrep[None, None, :])
        masked = jnp.where(amp_sym == 0, row_amps, 0.0)
        total = jnp.einsum("kac,kcjb->ajb", masked, masked_ints, precision=lax.Precision.HIGHEST)
        return total.reshape(V, J * V)

    return lax.map(one_row, (amplitudes, slab_irrep))
```

```python
import jax
import jax.numpy as jnp
from jax import lax
from jax.sharding import PartitionSpec as P


def per_device(amplitudes, cycle_integrals, occ_irrep, virt_irrep):
    slab_rows, occ_count, virt_count, c_local = amplitudes.shape
    col_count = lax.axis_size("col")
    row_count = lax.axis_size("row")
    k_local = occ_count // col_count
    a_local = virt_count // row_count
    column_slab = cycle_integrals.shape[2]
    col_place = lax.axis_index("col")
    row_place = lax.axis_index("row")
    k_irrep = lax.dynamic_slice_in_dim(occ_irrep, col_place * k_local, k_local)
    c_irrep = lax.dynamic_slice_in_dim(
        virt_irrep, (row_place * col_count + col_place) * c_local, c_local
    )
    slab_irrep = occ_irrep[:slab_rows]
    column_irrep = occ_irrep[:column_slab]
    int_sym = (
        k_irrep[:, None, None, None]
        ^ virt_irrep[None, :, None, None]
        ^ (column_irrep[None, None, :, None] ^ virt_irrep[None, None, None, :])
    )
    masked_ints = jnp.where(int_sym == 0, cycle_integrals, 0.0)

    chunks = 4 if slab_rows % 4 == 0 else 1
    rows = slab_rows // chunks
    results = []
    for step in range(chunks):
        amps = amplitudes[step * rows:(step + 1) * rows]
        amp_sym = (
            slab_irrep[step * rows:(step + 1) * rows, None, None, None]
            ^ occ_irrep[None, :, None, None]
            ^ (virt_irrep[None, None, :, None] ^ c_irrep[None, None, None, :])
        )
        masked_amps = jnp.where(amp_sym == 0, amps, 0.0)
        grouped = masked_amps.reshape(rows, col_count, k_local, row_count, a_local, c_local)
        grouped = jnp.transpose(grouped, (0, 3, 1, 2, 4, 5)).reshape(
            rows, row_count * col_count, k_local, a_local, c_local
        )
        items = lax.all_to_all(grouped, ("row", "col"), split_axis=1, concat_axis=4, tiled=True)
        blocks = items.reshape(rows, k_local, a_local, virt_count)
        partial_value = jnp.einsum(
            "ikac,kcjb->iajb",
            blocks,
            masked_ints,
            precision=lax.Precision.HIGH,
            preferred_element_type=jnp.float32,
        )
        flat = partial_value.reshape(rows, a_local, column_slab * virt_count)
        results.append(lax.psum_scatter(flat, "col", scatter_dimension=2, tiled=True))
    return jnp.concatenate(results, axis=0)


def solution(mesh):
    placed = (P(None, None, None, ("row", "col")), P("col", None, None, None), P(), P())
    return jax.shard_map(
        per_device, mesh=mesh, in_specs=placed, out_specs=P(None, "row", "col"), check_vma=False
    )
```

```python
import jax
import jax.numpy as jnp
from jax import lax
from jax.sharding import PartitionSpec as P


def chunk_plan(slab_rows):
    if slab_rows >= 8:
        head = slab_rows - 2
        sizes = [2] * (head // 2) + [1] * (head % 2) + [1, 1]
        return sizes
    return [1] * slab_rows


def per_device(amplitudes, cycle_integrals, occ_irrep, virt_irrep):
    slab_rows, occ_count, virt_count, c_local = amplitudes.shape
    col_count = lax.axis_size("col")
    row_count = lax.axis_size("row")
    k_local = occ_count // col_count
    a_local = virt_count // row_count
    column_slab = cycle_integrals.shape[2]
    col_place = lax.axis_index("col")
    row_place = lax.axis_index("row")
    k_irrep = lax.dynamic_slice_in_dim(occ_irrep, col_place * k_local, k_local)
    a_irrep = lax.dynamic_slice_in_dim(virt_irrep, row_place * a_local, a_local)
    slab_irrep = occ_irrep[:slab_rows]
    column_irrep = occ_irrep[:column_slab]
    int_sym = (
        k_irrep[:, None, None, None]
        ^ virt_irrep[None, :, None, None]
        ^ (column_irrep[None, None, :, None] ^ virt_irrep[None, None, None, :])
    )
    masked_ints = jnp.where(int_sym == 0, cycle_integrals, 0.0)

    results = []
    start = 0
    for step, rows in enumerate(chunk_plan(slab_rows)):
        amps = amplitudes[start:start + rows]
        grouped = amps.reshape(rows, col_count, k_local, row_count, a_local, c_local)
        grouped = jnp.transpose(grouped, (0, 3, 1, 2, 4, 5)).reshape(
            rows, row_count * col_count, k_local, a_local, c_local
        )
        if step == 1:
            grouped, masked_ints = lax.optimization_barrier((grouped, masked_ints))
        if step >= 2:
            grouped, results[step - 2] = lax.optimization_barrier((grouped, results[step - 2]))
        items = lax.all_to_all(grouped, ("row", "col"), split_axis=1, concat_axis=4, tiled=True)
        blocks = items.reshape(rows, k_local, a_local, virt_count)
        amp_sym = (
            slab_irrep[start:start + rows, None, None, None]
            ^ k_irrep[None, :, None, None]
            ^ (a_irrep[None, None, :, None] ^ virt_irrep[None, None, None, :])
        )
        blocks = jnp.where(amp_sym == 0, blocks, 0.0)
        partial_value = jnp.einsum(
            "ikac,kcjb->iajb",
            blocks,
            masked_ints,
            precision=lax.Precision.HIGH,
            preferred_element_type=jnp.float32,
        )
        flat = partial_value.reshape(rows, a_local, column_slab * virt_count)
        results.append(lax.psum_scatter(flat, "col", scatter_dimension=2, tiled=True))
        start += rows
    return jnp.concatenate(results, axis=0)


def solution(mesh):
    placed = (P(None, None, None, ("row", "col")), P("col", None, None, None), P(), P())
    return jax.shard_map(
        per_device, mesh=mesh, in_specs=placed, out_specs=P(None, "row", "col"), check_vma=False
    )
```

```python
import jax
import jax.numpy as jnp
from jax import lax
from jax.sharding import PartitionSpec as P


def per_device(amplitudes, cycle_integrals, occ_irrep, virt_irrep):
    slab_rows, occ_count, virt_count, c_local = amplitudes.shape
    col_count = lax.axis_size("col")
    row_count = lax.axis_size("row")
    k_local = occ_count // col_count
    a_local = virt_count // row_count
    column_slab = cycle_integrals.shape[2]
    col_place = lax.axis_index("col")
    row_place = lax.axis_index("row")
    k_irrep = lax.dynamic_slice_in_dim(occ_irrep, col_place * k_local, k_local)
    c_irrep = lax.dynamic_slice_in_dim(
        virt_irrep, (row_place * col_count + col_place) * c_local, c_local
    )
    slab_irrep = occ_irrep[:slab_rows]
    column_irrep = occ_irrep[:column_slab]
    int_sym = (
        k_irrep[:, None, None, None]
        ^ virt_irrep[None, :, None, None]
        ^ (column_irrep[None, None, :, None] ^ virt_irrep[None, None, None, :])
    )
    masked_ints = jnp.where(int_sym == 0, cycle_integrals, 0.0)

    rows = 1
    chunks = slab_rows // rows

    def prepare(step):
        amps = lax.dynamic_slice_in_dim(amplitudes, step * rows, rows, axis=0)
        row_irrep = lax.dynamic_slice_in_dim(slab_irrep, step * rows, rows)
        amp_sym = (
            row_irrep[:, None, None, None]
            ^ occ_irrep[None, :, None, None]
            ^ (virt_irrep[None, None, :, None] ^ c_irrep[None, None, None, :])
        )
        masked_amps = jnp.where(amp_sym == 0, amps, 0.0)
        grouped = masked_amps.reshape(rows, col_count, k_local, row_count, a_local, c_local)
        return jnp.transpose(grouped, (0, 3, 1, 2, 4, 5)).reshape(
            rows, row_count * col_count, k_local, a_local, c_local
        )

    def exchange(grouped):
        return lax.all_to_all(grouped, ("row", "col"), split_axis=1, concat_axis=4, tiled=True)

    def contract(items):
        blocks = items.reshape(rows, k_local, a_local, virt_count)
        partial_value = jnp.einsum(
            "ikac,kcjb->iajb",
            blocks,
            masked_ints,
            precision=lax.Precision.HIGH,
            preferred_element_type=jnp.float32,
        )
        flat = partial_value.reshape(rows, a_local, column_slab * virt_count)
        return lax.psum_scatter(flat, "col", scatter_dimension=2, tiled=True)

    out = jnp.zeros((slab_rows, a_local, column_slab * virt_count // col_count), jnp.float32)
    received = exchange(prepare(0))
    upcoming = prepare(min(1, chunks - 1))

    def body(step, carry):
        received, upcoming, out = carry
        next_received = exchange(upcoming)
        next_upcoming = prepare(jnp.minimum(step + 2, chunks - 1))
        out = lax.dynamic_update_slice_in_dim(out, contract(received), step * rows, axis=0)
        return next_received, next_upcoming, out

    received, upcoming, out = lax.fori_loop(0, chunks - 1, body, (received, upcoming, out))
    return lax.dynamic_update_slice_in_dim(out, contract(received), (chunks - 1) * rows, axis=0)


def solution(mesh):
    placed = (P(None, None, None, ("row", "col")), P("col", None, None, None), P(), P())
    return jax.shard_map(
        per_device, mesh=mesh, in_specs=placed, out_specs=P(None, "row", "col"), check_vma=False
    )
```

```python
import jax
import jax.numpy as jnp
from jax import lax
from jax.sharding import PartitionSpec as P


def per_device(amplitudes, cycle_integrals, occ_irrep, virt_irrep):
    slab_rows, occ_count, virt_count, c_local = amplitudes.shape
    col_count = lax.axis_size("col")
    row_count = lax.axis_size("row")
    k_local = occ_count // col_count
    a_local = virt_count // row_count
    column_slab = cycle_integrals.shape[2]
    col_place = lax.axis_index("col")
    row_place = lax.axis_index("row")
    k_irrep = lax.dynamic_slice_in_dim(occ_irrep, col_place * k_local, k_local)
    c_irrep = lax.dynamic_slice_in_dim(
        virt_irrep, (row_place * col_count + col_place) * c_local, c_local
    )
    slab_irrep = occ_irrep[:slab_rows]
    column_irrep = occ_irrep[:column_slab]
    int_sym = (
        k_irrep[:, None, None, None]
        ^ virt_irrep[None, :, None, None]
        ^ (column_irrep[None, None, :, None] ^ virt_irrep[None, None, None, :])
    )
    masked_ints = jnp.where(int_sym == 0, cycle_integrals, 0.0).reshape(
        k_local * virt_count, column_slab * virt_count
    )

    chunks = 4 if slab_rows % 4 == 0 else 1
    rows = slab_rows // chunks
    partials = []
    for step in range(chunks):
        amps = amplitudes[step * rows:(step + 1) * rows]
        amp_sym = (
            slab_irrep[step * rows:(step + 1) * rows, None, None, None]
            ^ occ_irrep[None, :, None, None]
            ^ (virt_irrep[None, None, :, None] ^ c_irrep[None, None, None, :])
        )
        masked_amps = jnp.where(amp_sym == 0, amps, 0.0)
        grouped = masked_amps.reshape(rows, col_count, k_local, row_count, a_local, c_local)
        grouped = jnp.transpose(grouped, (0, 3, 1, 2, 4, 5)).reshape(
            rows, row_count * col_count, k_local, a_local, c_local
        )
        if step == 1:
            grouped, masked_ints = lax.optimization_barrier((grouped, masked_ints))
        if step >= 2:
            grouped, partials[step - 2] = lax.optimization_barrier((grouped, partials[step - 2]))
        items = lax.all_to_all(grouped, ("row", "col"), split_axis=1, concat_axis=4, tiled=True)
        blocks = jnp.transpose(items.reshape(rows, k_local, a_local, virt_count), (0, 2, 1, 3))
        blocks = blocks.reshape(rows, a_local, k_local * virt_count)
        partial_value = jnp.einsum(
            "iap,pq->iaq",
            blocks,
            masked_ints,
            precision=lax.Precision.HIGH,
            preferred_element_type=jnp.float32,
        )
        partials.append(partial_value.reshape(rows, a_local, column_slab * virt_count))
    results = [lax.psum_scatter(flat, "col", scatter_dimension=2, tiled=True) for flat in partials]
    return jnp.concatenate(results, axis=0)


def solution(mesh):
    placed = (P(None, None, None, ("row", "col")), P("col", None, None, None), P(), P())
    return jax.shard_map(
        per_device, mesh=mesh, in_specs=placed, out_specs=P(None, "row", "col"), check_vma=False
    )
```

```python
import jax
import jax.numpy as jnp
from jax import lax
from jax.sharding import PartitionSpec as P


def scatter_sum(flat, col_count, col_place):
    rows, a_local, width = flat.shape
    shard = width // col_count
    pairs_n = col_count // 2
    side = col_place % 2
    line = col_place // 2
    parts = flat.reshape(rows, a_local, pairs_n, 2, shard)
    keep = jnp.where(side == 0, parts[:, :, :, 0], parts[:, :, :, 1])
    give = jnp.where(side == 0, parts[:, :, :, 1], parts[:, :, :, 0])
    swap = [(q, q ^ 1) for q in range(col_count)]
    line_sum = keep + lax.ppermute(give, "col", swap)
    total = lax.dynamic_index_in_dim(line_sum, line, axis=2, keepdims=False)
    up_prev = None
    down_prev = None
    for t in range(pairs_n - 1):
        up_send = line_sum[:, :, t + 1:]
        down_send = line_sum[:, :, :pairs_n - 1 - t]
        if up_prev is not None:
            up_send = up_send + up_prev[:, :, 1:]
            down_send = down_send + down_prev[:, :, :-1]
        payload = jnp.where(line == t, up_send, down_send)
        links = []
        for v in range(2):
            links.append((2 * t + v, 2 * (t + 1) + v))
            links.append((2 * (pairs_n - 1 - t) + v, 2 * (pairs_n - 2 - t) + v))
        got = lax.ppermute(payload, "col", links)
        up_prev = jnp.where(line == t + 1, got, 0.0)
        down_prev = jnp.where(line == pairs_n - 2 - t, got, 0.0)
        total = total + up_prev[:, :, 0] + down_prev[:, :, -1]
    return total


def per_device(amplitudes, cycle_integrals, occ_irrep, virt_irrep):
    slab_rows, occ_count, virt_count, c_local = amplitudes.shape
    col_count = lax.axis_size("col")
    row_count = lax.axis_size("row")
    k_local = occ_count // col_count
    a_local = virt_count // row_count
    column_slab = cycle_integrals.shape[2]
    col_place = lax.axis_index("col")
    row_place = lax.axis_index("row")
    k_irrep = lax.dynamic_slice_in_dim(occ_irrep, col_place * k_local, k_local)
    c_irrep = lax.dynamic_slice_in_dim(
        virt_irrep, (row_place * col_count + col_place) * c_local, c_local
    )
    slab_irrep = occ_irrep[:slab_rows]
    column_irrep = occ_irrep[:column_slab]
    int_sym = (
        k_irrep[:, None, None, None]
        ^ virt_irrep[None, :, None, None]
        ^ (column_irrep[None, None, :, None] ^ virt_irrep[None, None, None, :])
    )
    masked_ints = jnp.where(int_sym == 0, cycle_integrals, 0.0).reshape(
        k_local * virt_count, column_slab * virt_count
    )

    chunks = 4 if slab_rows % 4 == 0 else 1
    rows = slab_rows // chunks
    partials = []
    for step in range(chunks):
        amps = amplitudes[step * rows:(step + 1) * rows]
        amp_sym = (
            slab_irrep[step * rows:(step + 1) * rows, None, None, None]
            ^ occ_irrep[None, :, None, None]
            ^ (virt_irrep[None, None, :, None] ^ c_irrep[None, None, None, :])
        )
        masked_amps = jnp.where(amp_sym == 0, amps, 0.0)
        grouped = masked_amps.reshape(rows, col_count, k_local, row_count, a_local, c_local)
        grouped = jnp.transpose(grouped, (0, 3, 1, 2, 4, 5)).reshape(
            rows, row_count * col_count, k_local, a_local, c_local
        )
        if step == 1:
            grouped, masked_ints = lax.optimization_barrier((grouped, masked_ints))
        if step >= 2:
            grouped, partials[step - 2] = lax.optimization_barrier((grouped, partials[step - 2]))
        items = lax.all_to_all(grouped, ("row", "col"), split_axis=1, concat_axis=4, tiled=True)
        blocks = jnp.transpose(items.reshape(rows, k_local, a_local, virt_count), (0, 2, 1, 3))
        blocks = blocks.reshape(rows, a_local, k_local * virt_count)
        partial_value = jnp.einsum(
            "iap,pq->iaq",
            blocks,
            masked_ints,
            precision=lax.Precision.HIGH,
            preferred_element_type=jnp.float32,
        )
        partials.append(partial_value.reshape(rows, a_local, column_slab * virt_count))
    if col_count % 4 == 0:
        results = [scatter_sum(flat, col_count, col_place) for flat in partials]
    else:
        results = [lax.psum_scatter(flat, "col", scatter_dimension=2, tiled=True) for flat in partials]
    return jnp.concatenate(results, axis=0)


def solution(mesh):
    placed = (P(None, None, None, ("row", "col")), P("col", None, None, None), P(), P())
    return jax.shard_map(
        per_device, mesh=mesh, in_specs=placed, out_specs=P(None, "row", "col"), check_vma=False
    )
```

```python
import jax
import jax.numpy as jnp
from jax import lax
from jax.sharding import PartitionSpec as P


def scatter_sum(flat, col_count, col_place):
    rows, a_local, width = flat.shape
    shard = width // col_count
    pairs_n = col_count // 2
    side = col_place % 2
    line = col_place // 2
    parts = flat.reshape(rows, a_local, pairs_n, 2, shard)
    keep = jnp.where(side == 0, parts[:, :, :, 0], parts[:, :, :, 1])
    give = jnp.where(side == 0, parts[:, :, :, 1], parts[:, :, :, 0])
    swap = [(q, q ^ 1) for q in range(col_count)]
    line_sum = keep + lax.ppermute(give, "col", swap)
    total = lax.dynamic_index_in_dim(line_sum, line, axis=2, keepdims=False)
    up_prev = None
    down_prev = None
    for t in range(pairs_n - 1):
        up_send = line_sum[:, :, t + 1:]
        down_send = line_sum[:, :, :pairs_n - 1 - t]
        if up_prev is not None:
            up_send = up_send + up_prev[:, :, 1:]
            down_send = down_send + down_prev[:, :, :-1]
        payload = jnp.where(line == t, up_send, down_send)
        links = []
        for v in range(2):
            links.append((2 * t + v, 2 * (t + 1) + v))
            links.append((2 * (pairs_n - 1 - t) + v, 2 * (pairs_n - 2 - t) + v))
        got = lax.ppermute(payload, "col", links)
        up_prev = jnp.where(line == t + 1, got, 0.0)
        down_prev = jnp.where(line == pairs_n - 2 - t, got, 0.0)
        total = total + up_prev[:, :, 0] + down_prev[:, :, -1]
    return total


def per_device(amplitudes, cycle_integrals, occ_irrep, virt_irrep):
    slab_rows, occ_count, virt_count, c_local = amplitudes.shape
    col_count = lax.axis_size("col")
    row_count = lax.axis_size("row")
    k_local = occ_count // col_count
    a_local = virt_count // row_count
    column_slab = cycle_integrals.shape[2]
    col_place = lax.axis_index("col")
    row_place = lax.axis_index("row")
    k_irrep = lax.dynamic_slice_in_dim(occ_irrep, col_place * k_local, k_local)
    c_irrep = lax.dynamic_slice_in_dim(
        virt_irrep, (row_place * col_count + col_place) * c_local, c_local
    )
    slab_irrep = occ_irrep[:slab_rows]
    column_irrep = occ_irrep[:column_slab]
    int_sym = (
        k_irrep[:, None, None, None]
        ^ virt_irrep[None, :, None, None]
        ^ (column_irrep[None, None, :, None] ^ virt_irrep[None, None, None, :])
    )
    masked_ints = jnp.where(int_sym == 0, cycle_integrals, 0.0).reshape(
        k_local * virt_count, column_slab * virt_count
    )

    chunks = 4 if slab_rows % 4 == 0 else 1
    rows = slab_rows // chunks
    results = []
    for step in range(chunks):
        amps = amplitudes[step * rows:(step + 1) * rows]
        amp_sym = (
            slab_irrep[step * rows:(step + 1) * rows, None, None, None]
            ^ occ_irrep[None, :, None, None]
            ^ (virt_irrep[None, None, :, None] ^ c_irrep[None, None, None, :])
        )
        masked_amps = jnp.where(amp_sym == 0, amps, 0.0)
        grouped = masked_amps.reshape(rows, col_count, k_local, row_count, a_local, c_local)
        grouped = jnp.transpose(grouped, (0, 3, 1, 2, 4, 5)).reshape(
            rows, row_count * col_count, k_local, a_local, c_local
        )
        if step == 1:
            grouped, masked_ints = lax.optimization_barrier((grouped, masked_ints))
        if step >= 2:
            grouped, results[step - 2] = lax.optimization_barrier((grouped, results[step - 2]))
        items = lax.all_to_all(grouped, ("row", "col"), split_axis=1, concat_axis=4, tiled=True)
        blocks = jnp.transpose(items.reshape(rows, k_local, a_local, virt_count), (0, 2, 1, 3))
        blocks = blocks.reshape(rows, a_local, k_local * virt_count)
        partial_value = jnp.einsum(
            "iap,pq->iaq",
            blocks,
            masked_ints,
            precision=lax.Precision.HIGH,
            preferred_element_type=jnp.float32,
        )
        flat = partial_value.reshape(rows, a_local, column_slab * virt_count)
        if col_count % 4 == 0:
            results.append(scatter_sum(flat, col_count, col_place))
        else:
            results.append(lax.psum_scatter(flat, "col", scatter_dimension=2, tiled=True))
    return jnp.concatenate(results, axis=0)


def solution(mesh):
    placed = (P(None, None, None, ("row", "col")), P("col", None, None, None), P(), P())
    return jax.shard_map(
        per_device, mesh=mesh, in_specs=placed, out_specs=P(None, "row", "col"), check_vma=False
    )
```

```python
import jax
import jax.numpy as jnp
from jax import lax
from jax.sharding import PartitionSpec as P


def scatter_sum(flat, col_count, col_place):
    rows, a_local, width = flat.shape
    shard = width // col_count
    pairs_n = col_count // 2
    side = col_place % 2
    line = col_place // 2
    parts = flat.reshape(rows, a_local, pairs_n, 2, shard)
    keep = jnp.where(side == 0, parts[:, :, :, 0], parts[:, :, :, 1])
    give = jnp.where(side == 0, parts[:, :, :, 1], parts[:, :, :, 0])
    swap = [(q, q ^ 1) for q in range(col_count)]
    line_sum = keep + lax.ppermute(give, "col", swap)
    total = lax.dynamic_index_in_dim(line_sum, line, axis=2, keepdims=False)
    up_prev = None
    down_prev = None
    for t in range(pairs_n - 1):
        up_send = line_sum[:, :, t + 1:]
        down_send = line_sum[:, :, :pairs_n - 1 - t]
        if up_prev is not None:
            up_send = up_send + up_prev[:, :, 1:]
            down_send = down_send + down_prev[:, :, :-1]
        payload = jnp.where(line == t, up_send, down_send)
        links = []
        for v in range(2):
            links.append((2 * t + v, 2 * (t + 1) + v))
            links.append((2 * (pairs_n - 1 - t) + v, 2 * (pairs_n - 2 - t) + v))
        got = lax.ppermute(payload, "col", links)
        up_prev = jnp.where(line == t + 1, got, 0.0)
        down_prev = jnp.where(line == pairs_n - 2 - t, got, 0.0)
        total = total + up_prev[:, :, 0] + down_prev[:, :, -1]
    return total


def per_device(amplitudes, cycle_integrals, occ_irrep, virt_irrep):
    slab_rows, occ_count, virt_count, c_local = amplitudes.shape
    col_count = lax.axis_size("col")
    row_count = lax.axis_size("row")
    k_local = occ_count // col_count
    a_local = virt_count // row_count
    column_slab = cycle_integrals.shape[2]
    col_place = lax.axis_index("col")
    row_place = lax.axis_index("row")
    k_irrep = lax.dynamic_slice_in_dim(occ_irrep, col_place * k_local, k_local)
    c_irrep = lax.dynamic_slice_in_dim(
        virt_irrep, (row_place * col_count + col_place) * c_local, c_local
    )
    slab_irrep = occ_irrep[:slab_rows]
    column_irrep = occ_irrep[:column_slab]
    int_sym = (
        k_irrep[:, None, None, None]
        ^ virt_irrep[None, :, None, None]
        ^ (column_irrep[None, None, :, None] ^ virt_irrep[None, None, None, :])
    )
    masked_ints = jnp.where(int_sym == 0, cycle_integrals, 0.0).reshape(
        k_local * virt_count, column_slab * virt_count
    )

    chunks = 2 if slab_rows % 2 == 0 else 1
    rows = slab_rows // chunks
    results = []
    for step in range(chunks):
        amps = amplitudes[step * rows:(step + 1) * rows]
        amp_sym = (
            slab_irrep[step * rows:(step + 1) * rows, None, None, None]
            ^ occ_irrep[None, :, None, None]
            ^ (virt_irrep[None, None, :, None] ^ c_irrep[None, None, None, :])
        )
        masked_amps = jnp.where(amp_sym == 0, amps, 0.0)
        grouped = masked_amps.reshape(rows, col_count, k_local, row_count, a_local, c_local)
        grouped = jnp.transpose(grouped, (0, 3, 1, 2, 4, 5)).reshape(
            rows, row_count * col_count, k_local, a_local, c_local
        )
        if step == 1 and chunks > 2:
            grouped, masked_ints = lax.optimization_barrier((grouped, masked_ints))
        if step >= 2:
            grouped, results[step - 2] = lax.optimization_barrier((grouped, results[step - 2]))
        items = lax.all_to_all(grouped, ("row", "col"), split_axis=1, concat_axis=4, tiled=True)
        blocks = jnp.transpose(items.reshape(rows, k_local, a_local, virt_count), (0, 2, 1, 3))
        blocks = blocks.reshape(rows, a_local, k_local * virt_count)
        partial_value = jnp.einsum(
            "iap,pq->iaq",
            blocks,
            masked_ints,
            precision=lax.Precision.HIGH,
            preferred_element_type=jnp.float32,
        )
        flat = partial_value.reshape(rows, a_local, column_slab * virt_count)
        results.append(lax.psum_scatter(flat, "col", scatter_dimension=2, tiled=True))
    return jnp.concatenate(results, axis=0)


def solution(mesh):
    placed = (P(None, None, None, ("row", "col")), P("col", None, None, None), P(), P())
    return jax.shard_map(
        per_device, mesh=mesh, in_specs=placed, out_specs=P(None, "row", "col"), check_vma=False
    )
```

```python
import jax
import jax.numpy as jnp
from jax import lax
from jax.sharding import PartitionSpec as P


def scatter_sum(flat, col_count, col_place):
    rows, a_local, width = flat.shape
    shard = width // col_count
    pairs_n = col_count // 2
    side = col_place % 2
    line = col_place // 2
    parts = flat.reshape(rows, a_local, pairs_n, 2, shard)
    keep = jnp.where(side == 0, parts[:, :, :, 0], parts[:, :, :, 1])
    give = jnp.where(side == 0, parts[:, :, :, 1], parts[:, :, :, 0])
    swap = [(q, q ^ 1) for q in range(col_count)]
    line_sum = keep + lax.ppermute(give, "col", swap)
    total = lax.dynamic_index_in_dim(line_sum, line, axis=2, keepdims=False)
    up_prev = None
    down_prev = None
    for t in range(pairs_n - 1):
        up_send = line_sum[:, :, t + 1:]
        down_send = line_sum[:, :, :pairs_n - 1 - t]
        if up_prev is not None:
            up_send = up_send + up_prev[:, :, 1:]
            down_send = down_send + down_prev[:, :, :-1]
        payload = jnp.where(line == t, up_send, down_send)
        links = []
        for v in range(2):
            links.append((2 * t + v, 2 * (t + 1) + v))
            links.append((2 * (pairs_n - 1 - t) + v, 2 * (pairs_n - 2 - t) + v))
        got = lax.ppermute(payload, "col", links)
        up_prev = jnp.where(line == t + 1, got, 0.0)
        down_prev = jnp.where(line == pairs_n - 2 - t, got, 0.0)
        total = total + up_prev[:, :, 0] + down_prev[:, :, -1]
    return total


def per_device(amplitudes, cycle_integrals, occ_irrep, virt_irrep):
    slab_rows, occ_count, virt_count, c_local = amplitudes.shape
    col_count = lax.axis_size("col")
    row_count = lax.axis_size("row")
    k_local = occ_count // col_count
    a_local = virt_count // row_count
    column_slab = cycle_integrals.shape[2]
    col_place = lax.axis_index("col")
    row_place = lax.axis_index("row")
    k_irrep = lax.dynamic_slice_in_dim(occ_irrep, col_place * k_local, k_local)
    c_irrep = lax.dynamic_slice_in_dim(
        virt_irrep, (row_place * col_count + col_place) * c_local, c_local
    )
    slab_irrep = occ_irrep[:slab_rows]
    column_irrep = occ_irrep[:column_slab]
    int_sym = (
        k_irrep[:, None, None, None]
        ^ virt_irrep[None, :, None, None]
        ^ (column_irrep[None, None, :, None] ^ virt_irrep[None, None, None, :])
    )
    masked_ints = jnp.where(int_sym == 0, cycle_integrals, 0.0).reshape(
        k_local * virt_count, column_slab * virt_count
    )

    first = min(slab_rows, (slab_rows * 5 + 7) // 8)
    bounds = [(0, first)] + ([(first, slab_rows)] if first < slab_rows else [])
    chunks = len(bounds)
    exchanged = []
    for step, (lo, hi) in enumerate(bounds):
        rows = hi - lo
        amps = amplitudes[lo:hi]
        amp_sym = (
            slab_irrep[lo:hi, None, None, None]
            ^ occ_irrep[None, :, None, None]
            ^ (virt_irrep[None, None, :, None] ^ c_irrep[None, None, None, :])
        )
        masked_amps = jnp.where(amp_sym == 0, amps, 0.0)
        grouped = masked_amps.reshape(rows, col_count, k_local, row_count, a_local, c_local)
        grouped = jnp.transpose(grouped, (0, 3, 1, 2, 4, 5)).reshape(
            rows, row_count * col_count, k_local, a_local, c_local
        )
        if step == 1:
            grouped, exchanged[0], masked_ints = lax.optimization_barrier(
                (grouped, exchanged[0], masked_ints)
            )
        exchanged.append(
            lax.all_to_all(grouped, ("row", "col"), split_axis=1, concat_axis=4, tiled=True)
        )
    results = []
    for items in exchanged:
        rows = items.shape[0]
        blocks = jnp.transpose(items.reshape(rows, k_local, a_local, virt_count), (0, 2, 1, 3))
        blocks = blocks.reshape(rows, a_local, k_local * virt_count)
        partial_value = jnp.einsum(
            "iap,pq->iaq",
            blocks,
            masked_ints,
            precision=lax.Precision.HIGH,
            preferred_element_type=jnp.float32,
        )
        flat = partial_value.reshape(rows, a_local, column_slab * virt_count)
        results.append(lax.psum_scatter(flat, "col", scatter_dimension=2, tiled=True))
    return jnp.concatenate(results, axis=0)


def solution(mesh):
    placed = (P(None, None, None, ("row", "col")), P("col", None, None, None), P(), P())
    return jax.shard_map(
        per_device, mesh=mesh, in_specs=placed, out_specs=P(None, "row", "col"), check_vma=False
    )
```

```python
import jax
import jax.numpy as jnp
from jax import lax
from jax.sharding import PartitionSpec as P


def scatter_sum(flat, col_count, col_place):
    rows, a_local, width = flat.shape
    shard = width // col_count
    pairs_n = col_count // 2
    side = col_place % 2
    line = col_place // 2
    parts = flat.reshape(rows, a_local, pairs_n, 2, shard)
    keep = jnp.where(side == 0, parts[:, :, :, 0], parts[:, :, :, 1])
    give = jnp.where(side == 0, parts[:, :, :, 1], parts[:, :, :, 0])
    swap = [(q, q ^ 1) for q in range(col_count)]
    line_sum = keep + lax.ppermute(give, "col", swap)
    total = lax.dynamic_index_in_dim(line_sum, line, axis=2, keepdims=False)
    up_prev = None
    down_prev = None
    for t in range(pairs_n - 1):
        up_send = line_sum[:, :, t + 1:]
        down_send = line_sum[:, :, :pairs_n - 1 - t]
        if up_prev is not None:
            up_send = up_send + up_prev[:, :, 1:]
            down_send = down_send + down_prev[:, :, :-1]
        payload = jnp.where(line == t, up_send, down_send)
        links = []
        for v in range(2):
            links.append((2 * t + v, 2 * (t + 1) + v))
            links.append((2 * (pairs_n - 1 - t) + v, 2 * (pairs_n - 2 - t) + v))
        got = lax.ppermute(payload, "col", links)
        up_prev = jnp.where(line == t + 1, got, 0.0)
        down_prev = jnp.where(line == pairs_n - 2 - t, got, 0.0)
        total = total + up_prev[:, :, 0] + down_prev[:, :, -1]
    return total


def per_device(amplitudes, cycle_integrals, occ_irrep, virt_irrep):
    slab_rows, occ_count, virt_count, c_local = amplitudes.shape
    col_count = lax.axis_size("col")
    row_count = lax.axis_size("row")
    k_local = occ_count // col_count
    a_local = virt_count // row_count
    column_slab = cycle_integrals.shape[2]
    col_place = lax.axis_index("col")
    row_place = lax.axis_index("row")
    k_irrep = lax.dynamic_slice_in_dim(occ_irrep, col_place * k_local, k_local)
    c_irrep = lax.dynamic_slice_in_dim(
        virt_irrep, (row_place * col_count + col_place) * c_local, c_local
    )
    slab_irrep = occ_irrep[:slab_rows]
    column_irrep = occ_irrep[:column_slab]
    int_sym = (
        k_irrep[:, None, None, None]
        ^ virt_irrep[None, :, None, None]
        ^ (column_irrep[None, None, :, None] ^ virt_irrep[None, None, None, :])
    )
    masked_ints = jnp.where(int_sym == 0, cycle_integrals, 0.0).reshape(
        k_local * virt_count, column_slab * virt_count
    )

    chunks = 2 if slab_rows % 2 == 0 else 1
    rows = slab_rows // chunks
    results = []
    for step in range(chunks):
        amps = amplitudes[step * rows:(step + 1) * rows]
        amp_sym = (
            slab_irrep[step * rows:(step + 1) * rows, None, None, None]
            ^ occ_irrep[None, :, None, None]
            ^ (virt_irrep[None, None, :, None] ^ c_irrep[None, None, None, :])
        )
        masked_amps = jnp.where(amp_sym == 0, amps, 0.0)
        grouped = masked_amps.reshape(rows, col_count, k_local, row_count, a_local, c_local)
        grouped = jnp.transpose(grouped, (0, 3, 1, 2, 4, 5)).reshape(
            rows, row_count * col_count, k_local, a_local, c_local
        )
        if step == 1 and chunks > 2:
            grouped, masked_ints = lax.optimization_barrier((grouped, masked_ints))
        if step >= 2:
            grouped, results[step - 2] = lax.optimization_barrier((grouped, results[step - 2]))
        items = lax.all_to_all(grouped, ("row", "col"), split_axis=1, concat_axis=4, tiled=True)
        blocks = jnp.transpose(items.reshape(rows, k_local, a_local, virt_count), (0, 2, 1, 3))
        blocks = blocks.reshape(rows, a_local, k_local * virt_count)
        partial_value = jnp.einsum(
            "iap,pq->iaq",
            blocks,
            masked_ints,
            precision=lax.Precision.HIGH,
            preferred_element_type=jnp.float32,
        )
        flat = partial_value.reshape(rows, a_local, column_slab * virt_count)
        if step == chunks - 1 and rows % 2 == 0 and col_count % 4 == 0:
            half = rows // 2
            results.append(
                jnp.concatenate(
                    [
                        lax.psum_scatter(flat[:half], "col", scatter_dimension=2, tiled=True),
                        scatter_sum(flat[half:], col_count, col_place),
                    ],
                    axis=0,
                )
            )
        else:
            results.append(lax.psum_scatter(flat, "col", scatter_dimension=2, tiled=True))
    return jnp.concatenate(results, axis=0)


def solution(mesh):
    placed = (P(None, None, None, ("row", "col")), P("col", None, None, None), P(), P())
    return jax.shard_map(
        per_device, mesh=mesh, in_specs=placed, out_specs=P(None, "row", "col"), check_vma=False
    )
```

```python
import jax
import jax.numpy as jnp
from jax import lax
from jax.sharding import PartitionSpec as P


def scatter_sum(flat, col_count, col_place):
    rows, a_local, width = flat.shape
    shard = width // col_count
    pairs_n = col_count // 2
    side = col_place % 2
    line = col_place // 2
    parts = flat.reshape(rows, a_local, pairs_n, 2, shard)
    keep = jnp.where(side == 0, parts[:, :, :, 0], parts[:, :, :, 1])
    give = jnp.where(side == 0, parts[:, :, :, 1], parts[:, :, :, 0])
    swap = [(q, q ^ 1) for q in range(col_count)]
    line_sum = keep + lax.ppermute(give, "col", swap)
    total = lax.dynamic_index_in_dim(line_sum, line, axis=2, keepdims=False)
    up_prev = None
    down_prev = None
    for t in range(pairs_n - 1):
        up_send = line_sum[:, :, t + 1:]
        down_send = line_sum[:, :, :pairs_n - 1 - t]
        if up_prev is not None:
            up_send = up_send + up_prev[:, :, 1:]
            down_send = down_send + down_prev[:, :, :-1]
        payload = jnp.where(line == t, up_send, down_send)
        links = []
        for v in range(2):
            links.append((2 * t + v, 2 * (t + 1) + v))
            links.append((2 * (pairs_n - 1 - t) + v, 2 * (pairs_n - 2 - t) + v))
        got = lax.ppermute(payload, "col", links)
        up_prev = jnp.where(line == t + 1, got, 0.0)
        down_prev = jnp.where(line == pairs_n - 2 - t, got, 0.0)
        total = total + up_prev[:, :, 0] + down_prev[:, :, -1]
    return total


def per_device(amplitudes, cycle_integrals, occ_irrep, virt_irrep):
    slab_rows, occ_count, virt_count, c_local = amplitudes.shape
    col_count = lax.axis_size("col")
    row_count = lax.axis_size("row")
    k_local = occ_count // col_count
    a_local = virt_count // row_count
    column_slab = cycle_integrals.shape[2]
    col_place = lax.axis_index("col")
    row_place = lax.axis_index("row")
    k_irrep = lax.dynamic_slice_in_dim(occ_irrep, col_place * k_local, k_local)
    c_irrep = lax.dynamic_slice_in_dim(
        virt_irrep, (row_place * col_count + col_place) * c_local, c_local
    )
    slab_irrep = occ_irrep[:slab_rows]
    column_irrep = occ_irrep[:column_slab]
    int_sym = (
        k_irrep[:, None, None, None]
        ^ virt_irrep[None, :, None, None]
        ^ (column_irrep[None, None, :, None] ^ virt_irrep[None, None, None, :])
    )
    masked_ints = jnp.where(int_sym == 0, cycle_integrals, 0.0).reshape(
        k_local * virt_count, column_slab * virt_count
    )

    first = min(slab_rows, (slab_rows + 1) // 2)
    bounds = [(0, first)] + ([(first, slab_rows)] if first < slab_rows else [])
    chunks = len(bounds)
    exchanged = []
    for step, (lo, hi) in enumerate(bounds):
        rows = hi - lo
        amps = amplitudes[lo:hi]
        amp_sym = (
            slab_irrep[lo:hi, None, None, None]
            ^ occ_irrep[None, :, None, None]
            ^ (virt_irrep[None, None, :, None] ^ c_irrep[None, None, None, :])
        )
        masked_amps = jnp.where(amp_sym == 0, amps, 0.0)
        grouped = masked_amps.reshape(rows, col_count, k_local, row_count, a_local, c_local)
        grouped = jnp.transpose(grouped, (0, 3, 1, 2, 4, 5)).reshape(
            rows, row_count * col_count, k_local, a_local, c_local
        )
        if step == 1:
            grouped, exchanged[0], masked_ints = lax.optimization_barrier(
                (grouped, exchanged[0], masked_ints)
            )
        exchanged.append(
            lax.all_to_all(grouped, ("row", "col"), split_axis=1, concat_axis=4, tiled=True)
        )
    results = []
    for step, items in enumerate(exchanged):
        rows = items.shape[0]
        if step >= 1:
            items, results[step - 1] = lax.optimization_barrier((items, results[step - 1]))
        blocks = jnp.transpose(items.reshape(rows, k_local, a_local, virt_count), (0, 2, 1, 3))
        blocks = blocks.reshape(rows, a_local, k_local * virt_count)
        partial_value = jnp.einsum(
            "iap,pq->iaq",
            blocks,
            masked_ints,
            precision=lax.Precision.HIGH,
            preferred_element_type=jnp.float32,
        )
        flat = partial_value.reshape(rows, a_local, column_slab * virt_count)
        if step < chunks - 1 and col_count % 4 == 0:
            results.append(scatter_sum(flat, col_count, col_place))
        else:
            results.append(lax.psum_scatter(flat, "col", scatter_dimension=2, tiled=True))
    return jnp.concatenate(results, axis=0)


def solution(mesh):
    placed = (P(None, None, None, ("row", "col")), P("col", None, None, None), P(), P())
    return jax.shard_map(
        per_device, mesh=mesh, in_specs=placed, out_specs=P(None, "row", "col"), check_vma=False
    )
```

```python
import jax
import jax.numpy as jnp
from jax import lax
from jax.sharding import PartitionSpec as P


def scatter_sum(flat, col_count, col_place):
    rows, a_local, width = flat.shape
    shard = width // col_count
    pairs_n = col_count // 2
    side = col_place % 2
    line = col_place // 2
    parts = flat.reshape(rows, a_local, pairs_n, 2, shard)
    keep = jnp.where(side == 0, parts[:, :, :, 0], parts[:, :, :, 1])
    give = jnp.where(side == 0, parts[:, :, :, 1], parts[:, :, :, 0])
    swap = [(q, q ^ 1) for q in range(col_count)]
    line_sum = keep + lax.ppermute(give, "col", swap)
    total = lax.dynamic_index_in_dim(line_sum, line, axis=2, keepdims=False)
    up_prev = None
    down_prev = None
    for t in range(pairs_n - 1):
        up_send = line_sum[:, :, t + 1:]
        down_send = line_sum[:, :, :pairs_n - 1 - t]
        if up_prev is not None:
            up_send = up_send + up_prev[:, :, 1:]
            down_send = down_send + down_prev[:, :, :-1]
        payload = jnp.where(line == t, up_send, down_send)
        links = []
        for v in range(2):
            links.append((2 * t + v, 2 * (t + 1) + v))
            links.append((2 * (pairs_n - 1 - t) + v, 2 * (pairs_n - 2 - t) + v))
        got = lax.ppermute(payload, "col", links)
        up_prev = jnp.where(line == t + 1, got, 0.0)
        down_prev = jnp.where(line == pairs_n - 2 - t, got, 0.0)
        total = total + up_prev[:, :, 0] + down_prev[:, :, -1]
    return total


def per_device(amplitudes, cycle_integrals, occ_irrep, virt_irrep):
    slab_rows, occ_count, virt_count, c_local = amplitudes.shape
    col_count = lax.axis_size("col")
    row_count = lax.axis_size("row")
    k_local = occ_count // col_count
    a_local = virt_count // row_count
    column_slab = cycle_integrals.shape[2]
    col_place = lax.axis_index("col")
    row_place = lax.axis_index("row")
    k_irrep = lax.dynamic_slice_in_dim(occ_irrep, col_place * k_local, k_local)
    c_irrep = lax.dynamic_slice_in_dim(
        virt_irrep, (row_place * col_count + col_place) * c_local, c_local
    )
    slab_irrep = occ_irrep[:slab_rows]
    column_irrep = occ_irrep[:column_slab]
    int_sym = (
        k_irrep[:, None, None, None]
        ^ virt_irrep[None, :, None, None]
        ^ (column_irrep[None, None, :, None] ^ virt_irrep[None, None, None, :])
    )
    masked_ints = jnp.where(int_sym == 0, cycle_integrals, 0.0).reshape(
        k_local * virt_count, column_slab * virt_count
    )

    first = (slab_rows * 3 + 7) // 8
    second = min(slab_rows, 2 * first)
    bounds = [(lo, hi) for lo, hi in ((0, first), (first, second), (second, slab_rows)) if hi > lo]
    chunks = len(bounds)
    results = []
    for step, (lo, hi) in enumerate(bounds):
        rows = hi - lo
        amps = amplitudes[lo:hi]
        amp_sym = (
            slab_irrep[lo:hi, None, None, None]
            ^ occ_irrep[None, :, None, None]
            ^ (virt_irrep[None, None, :, None] ^ c_irrep[None, None, None, :])
        )
        masked_amps = jnp.where(amp_sym == 0, amps, 0.0)
        grouped = masked_amps.reshape(rows, col_count, k_local, row_count, a_local, c_local)
        grouped = jnp.transpose(grouped, (0, 3, 1, 2, 4, 5)).reshape(
            rows, row_count * col_count, k_local, a_local, c_local
        )
        if step == 1 and chunks > 2:
            grouped, masked_ints = lax.optimization_barrier((grouped, masked_ints))
        if step >= 2:
            grouped, results[step - 2] = lax.optimization_barrier((grouped, results[step - 2]))
        items = lax.all_to_all(grouped, ("row", "col"), split_axis=1, concat_axis=4, tiled=True)
        blocks = jnp.transpose(items.reshape(rows, k_local, a_local, virt_count), (0, 2, 1, 3))
        blocks = blocks.reshape(rows, a_local, k_local * virt_count)
        partial_value = jnp.einsum(
            "iap,pq->iaq",
            blocks,
            masked_ints,
            precision=lax.Precision.HIGH,
            preferred_element_type=jnp.float32,
        )
        flat = partial_value.reshape(rows, a_local, column_slab * virt_count)
        results.append(lax.psum_scatter(flat, "col", scatter_dimension=2, tiled=True))
    return jnp.concatenate(results, axis=0)


def solution(mesh):
    placed = (P(None, None, None, ("row", "col")), P("col", None, None, None), P(), P())
    return jax.shard_map(
        per_device, mesh=mesh, in_specs=placed, out_specs=P(None, "row", "col"), check_vma=False
    )
```

```python
import jax
import jax.numpy as jnp
from jax import lax
from jax.sharding import PartitionSpec as P


def scatter_sum(flat, col_count, col_place):
    rows, a_local, width = flat.shape
    shard = width // col_count
    pairs_n = col_count // 2
    side = col_place % 2
    line = col_place // 2
    parts = flat.reshape(rows, a_local, pairs_n, 2, shard)
    keep = jnp.where(side == 0, parts[:, :, :, 0], parts[:, :, :, 1])
    give = jnp.where(side == 0, parts[:, :, :, 1], parts[:, :, :, 0])
    swap = [(q, q ^ 1) for q in range(col_count)]
    line_sum = keep + lax.ppermute(give, "col", swap)
    total = lax.dynamic_index_in_dim(line_sum, line, axis=2, keepdims=False)
    up_prev = None
    down_prev = None
    for t in range(pairs_n - 1):
        up_send = line_sum[:, :, t + 1:]
        down_send = line_sum[:, :, :pairs_n - 1 - t]
        if up_prev is not None:
            up_send = up_send + up_prev[:, :, 1:]
            down_send = down_send + down_prev[:, :, :-1]
        payload = jnp.where(line == t, up_send, down_send)
        links = []
        for v in range(2):
            links.append((2 * t + v, 2 * (t + 1) + v))
            links.append((2 * (pairs_n - 1 - t) + v, 2 * (pairs_n - 2 - t) + v))
        got = lax.ppermute(payload, "col", links)
        up_prev = jnp.where(line == t + 1, got, 0.0)
        down_prev = jnp.where(line == pairs_n - 2 - t, got, 0.0)
        total = total + up_prev[:, :, 0] + down_prev[:, :, -1]
    return total


def per_device(amplitudes, cycle_integrals, occ_irrep, virt_irrep):
    slab_rows, occ_count, virt_count, c_local = amplitudes.shape
    col_count = lax.axis_size("col")
    row_count = lax.axis_size("row")
    k_local = occ_count // col_count
    a_local = virt_count // row_count
    column_slab = cycle_integrals.shape[2]
    col_place = lax.axis_index("col")
    row_place = lax.axis_index("row")
    k_irrep = lax.dynamic_slice_in_dim(occ_irrep, col_place * k_local, k_local)
    a_irrep = lax.dynamic_slice_in_dim(virt_irrep, row_place * a_local, a_local)
    slab_irrep = occ_irrep[:slab_rows]
    column_irrep = occ_irrep[:column_slab]
    int_sym = (
        k_irrep[:, None, None, None]
        ^ virt_irrep[None, :, None, None]
        ^ (column_irrep[None, None, :, None] ^ virt_irrep[None, None, None, :])
    )
    masked_ints = jnp.where(int_sym == 0, cycle_integrals, 0.0).reshape(
        k_local * virt_count, column_slab * virt_count
    )

    chunks = 2 if slab_rows % 2 == 0 else 1
    rows = slab_rows // chunks
    results = []
    flats = []
    for step in range(chunks):
        amps = amplitudes[step * rows:(step + 1) * rows]
        grouped = amps.reshape(rows, col_count, k_local, row_count, a_local, c_local)
        grouped = jnp.transpose(grouped, (0, 3, 1, 2, 4, 5)).reshape(
            rows, row_count * col_count, k_local, a_local, c_local
        )
        if step == 1 and chunks > 2:
            grouped, masked_ints = lax.optimization_barrier((grouped, masked_ints))
        if step >= 2:
            grouped, results[step - 2] = lax.optimization_barrier((grouped, results[step - 2]))
        items = lax.all_to_all(grouped, ("row", "col"), split_axis=1, concat_axis=4, tiled=True)
        if step >= 1:
            items, results[step - 1] = lax.optimization_barrier((items, results[step - 1]))
        amp_sym = (
            slab_irrep[step * rows:(step + 1) * rows, None, None, None]
            ^ k_irrep[None, :, None, None]
            ^ (a_irrep[None, None, :, None] ^ virt_irrep[None, None, None, :])
        )
        blocks = jnp.where(amp_sym == 0, items.reshape(rows, k_local, a_local, virt_count), 0.0)
        blocks = jnp.transpose(blocks, (0, 2, 1, 3))
        blocks = blocks.reshape(rows, a_local, k_local * virt_count)
        partial_value = jnp.einsum(
            "iap,pq->iaq",
            blocks,
            masked_ints,
            precision=lax.Precision.HIGH,
            preferred_element_type=jnp.float32,
        )
        flat = partial_value.reshape(rows, a_local, column_slab * virt_count)
        flats.append(flat)
        results.append(lax.psum_scatter(flat, "col", scatter_dimension=2, tiled=True))
    return jnp.concatenate(results, axis=0)


def solution(mesh):
    placed = (P(None, None, None, ("row", "col")), P("col", None, None, None), P(), P())
    return jax.shard_map(
        per_device, mesh=mesh, in_specs=placed, out_specs=P(None, "row", "col"), check_vma=False
    )
```

```python
import jax
import jax.numpy as jnp
from jax import lax
from jax.sharding import PartitionSpec as P


def scatter_sum(flat, col_count, col_place):
    rows, a_local, width = flat.shape
    shard = width // col_count
    pairs_n = col_count // 2
    side = col_place % 2
    line = col_place // 2
    parts = flat.reshape(rows, a_local, pairs_n, 2, shard)
    keep = jnp.where(side == 0, parts[:, :, :, 0], parts[:, :, :, 1])
    give = jnp.where(side == 0, parts[:, :, :, 1], parts[:, :, :, 0])
    swap = [(q, q ^ 1) for q in range(col_count)]
    line_sum = keep + lax.ppermute(give, "col", swap)
    total = lax.dynamic_index_in_dim(line_sum, line, axis=2, keepdims=False)
    up_prev = None
    down_prev = None
    for t in range(pairs_n - 1):
        up_send = line_sum[:, :, t + 1:]
        down_send = line_sum[:, :, :pairs_n - 1 - t]
        if up_prev is not None:
            up_send = up_send + up_prev[:, :, 1:]
            down_send = down_send + down_prev[:, :, :-1]
        payload = jnp.where(line == t, up_send, down_send)
        links = []
        for v in range(2):
            links.append((2 * t + v, 2 * (t + 1) + v))
            links.append((2 * (pairs_n - 1 - t) + v, 2 * (pairs_n - 2 - t) + v))
        got = lax.ppermute(payload, "col", links)
        up_prev = jnp.where(line == t + 1, got, 0.0)
        down_prev = jnp.where(line == pairs_n - 2 - t, got, 0.0)
        total = total + up_prev[:, :, 0] + down_prev[:, :, -1]
    return total


def per_device(amplitudes, cycle_integrals, occ_irrep, virt_irrep):
    slab_rows, occ_count, virt_count, c_local = amplitudes.shape
    col_count = lax.axis_size("col")
    row_count = lax.axis_size("row")
    k_local = occ_count // col_count
    a_local = virt_count // row_count
    column_slab = cycle_integrals.shape[2]
    col_place = lax.axis_index("col")
    row_place = lax.axis_index("row")
    k_irrep = lax.dynamic_slice_in_dim(occ_irrep, col_place * k_local, k_local)
    c_irrep = lax.dynamic_slice_in_dim(
        virt_irrep, (row_place * col_count + col_place) * c_local, c_local
    )
    slab_irrep = occ_irrep[:slab_rows]
    column_irrep = occ_irrep[:column_slab]
    int_sym = (
        k_irrep[:, None, None, None]
        ^ virt_irrep[None, :, None, None]
        ^ (column_irrep[None, None, :, None] ^ virt_irrep[None, None, None, :])
    )
    masked_ints = jnp.where(int_sym == 0, cycle_integrals, 0.0).reshape(
        k_local * virt_count, column_slab * virt_count
    )

    first = (slab_rows * 2 + 7) // 8
    second = min(slab_rows, first + (slab_rows - first + 1) // 2)
    bounds = [(lo, hi) for lo, hi in ((0, first), (first, second), (second, slab_rows)) if hi > lo]
    chunks = len(bounds)
    results = []
    for step, (lo, hi) in enumerate(bounds):
        rows = hi - lo
        amps = amplitudes[lo:hi]
        amp_sym = (
            slab_irrep[lo:hi, None, None, None]
            ^ occ_irrep[None, :, None, None]
            ^ (virt_irrep[None, None, :, None] ^ c_irrep[None, None, None, :])
        )
        masked_amps = jnp.where(amp_sym == 0, amps, 0.0)
        grouped = masked_amps.reshape(rows, col_count, k_local, row_count, a_local, c_local)
        grouped = jnp.transpose(grouped, (0, 3, 1, 2, 4, 5)).reshape(
            rows, row_count * col_count, k_local, a_local, c_local
        )
        if step == 1 and chunks > 2:
            grouped, masked_ints = lax.optimization_barrier((grouped, masked_ints))
        if step >= 2:
            grouped, results[step - 2] = lax.optimization_barrier((grouped, results[step - 2]))
        items = lax.all_to_all(grouped, ("row", "col"), split_axis=1, concat_axis=4, tiled=True)
        blocks = jnp.transpose(items.reshape(rows, k_local, a_local, virt_count), (0, 2, 1, 3))
        blocks = blocks.reshape(rows, a_local, k_local * virt_count)
        partial_value = jnp.einsum(
            "iap,pq->iaq",
            blocks,
            masked_ints,
            precision=lax.Precision.HIGH,
            preferred_element_type=jnp.float32,
        )
        flat = partial_value.reshape(rows, a_local, column_slab * virt_count)
        results.append(lax.psum_scatter(flat, "col", scatter_dimension=2, tiled=True))
    return jnp.concatenate(results, axis=0)


def solution(mesh):
    placed = (P(None, None, None, ("row", "col")), P("col", None, None, None), P(), P())
    return jax.shard_map(
        per_device, mesh=mesh, in_specs=placed, out_specs=P(None, "row", "col"), check_vma=False
    )
```

```python
import jax
import jax.numpy as jnp
from jax import lax
from jax.sharding import PartitionSpec as P


def scatter_sum(flat, col_count, col_place):
    rows, a_local, width = flat.shape
    shard = width // col_count
    pairs_n = col_count // 2
    side = col_place % 2
    line = col_place // 2
    parts = flat.reshape(rows, a_local, pairs_n, 2, shard)
    keep = jnp.where(side == 0, parts[:, :, :, 0], parts[:, :, :, 1])
    give = jnp.where(side == 0, parts[:, :, :, 1], parts[:, :, :, 0])
    swap = [(q, q ^ 1) for q in range(col_count)]
    line_sum = keep + lax.ppermute(give, "col", swap)
    total = lax.dynamic_index_in_dim(line_sum, line, axis=2, keepdims=False)
    up_prev = None
    down_prev = None
    for t in range(pairs_n - 1):
        up_send = line_sum[:, :, t + 1:]
        down_send = line_sum[:, :, :pairs_n - 1 - t]
        if up_prev is not None:
            up_send = up_send + up_prev[:, :, 1:]
            down_send = down_send + down_prev[:, :, :-1]
        payload = jnp.where(line == t, up_send, down_send)
        links = []
        for v in range(2):
            links.append((2 * t + v, 2 * (t + 1) + v))
            links.append((2 * (pairs_n - 1 - t) + v, 2 * (pairs_n - 2 - t) + v))
        got = lax.ppermute(payload, "col", links)
        up_prev = jnp.where(line == t + 1, got, 0.0)
        down_prev = jnp.where(line == pairs_n - 2 - t, got, 0.0)
        total = total + up_prev[:, :, 0] + down_prev[:, :, -1]
    return total


def per_device(amplitudes, cycle_integrals, occ_irrep, virt_irrep):
    slab_rows, occ_count, virt_count, c_local = amplitudes.shape
    col_count = lax.axis_size("col")
    row_count = lax.axis_size("row")
    k_local = occ_count // col_count
    a_local = virt_count // row_count
    column_slab = cycle_integrals.shape[2]
    col_place = lax.axis_index("col")
    row_place = lax.axis_index("row")
    k_irrep = lax.dynamic_slice_in_dim(occ_irrep, col_place * k_local, k_local)
    c_irrep = lax.dynamic_slice_in_dim(
        virt_irrep, (row_place * col_count + col_place) * c_local, c_local
    )
    slab_irrep = occ_irrep[:slab_rows]
    column_irrep = occ_irrep[:column_slab]
    int_sym = (
        k_irrep[:, None, None, None]
        ^ virt_irrep[None, :, None, None]
        ^ (column_irrep[None, None, :, None] ^ virt_irrep[None, None, None, :])
    )
    masked_ints = jnp.where(int_sym == 0, cycle_integrals, 0.0).reshape(
        k_local * virt_count, column_slab * virt_count
    )

    first = (slab_rows * 2 + 7) // 8
    second = min(slab_rows, 2 * first)
    bounds = [(lo, hi) for lo, hi in ((0, first), (first, second), (second, slab_rows)) if hi > lo]
    chunks = len(bounds)
    results = []
    for step, (lo, hi) in enumerate(bounds):
        rows = hi - lo
        amps = amplitudes[lo:hi]
        amp_sym = (
            slab_irrep[lo:hi, None, None, None]
            ^ occ_irrep[None, :, None, None]
            ^ (virt_irrep[None, None, :, None] ^ c_irrep[None, None, None, :])
        )
        masked_amps = jnp.where(amp_sym == 0, amps, 0.0)
        grouped = masked_amps.reshape(rows, col_count, k_local, row_count, a_local, c_local)
        grouped = jnp.transpose(grouped, (0, 3, 1, 2, 4, 5)).reshape(
            rows, row_count * col_count, k_local, a_local, c_local
        )
        if step == 1 and chunks > 2:
            grouped, masked_ints = lax.optimization_barrier((grouped, masked_ints))
        if step >= 2:
            grouped, results[step - 2] = lax.optimization_barrier((grouped, results[step - 2]))
        items = lax.all_to_all(grouped, ("row", "col"), split_axis=1, concat_axis=4, tiled=True)
        blocks = jnp.transpose(items.reshape(rows, k_local, a_local, virt_count), (0, 2, 1, 3))
        blocks = blocks.reshape(rows, a_local, k_local * virt_count)
        partial_value = jnp.einsum(
            "iap,pq->iaq",
            blocks,
            masked_ints,
            precision=lax.Precision.HIGH,
            preferred_element_type=jnp.float32,
        )
        flat = partial_value.reshape(rows, a_local, column_slab * virt_count)
        results.append(lax.psum_scatter(flat, "col", scatter_dimension=2, tiled=True))
    return jnp.concatenate(results, axis=0)


def solution(mesh):
    placed = (P(None, None, None, ("row", "col")), P("col", None, None, None), P(), P())
    return jax.shard_map(
        per_device, mesh=mesh, in_specs=placed, out_specs=P(None, "row", "col"), check_vma=False
    )
```
